1024 devices in a mesh: seq: 128 (over y, z), head: 8 (over x, core).
Axes of the slice: x: 4, y: 4, z: 32, core: 2. Of those that a mesh axis runs over, the one named last changes fastest.
Arguments:
- queries: bfloat16 [16384, 8, 1024], P('seq', 'head'), may hold values from -6 to 6
- keys: bfloat16 [16384, 1024], P('seq', 'head'), may hold values from -6 to 6
- values: bfloat16 [16384, 1024], P('seq', 'head'), may hold values from -6 to 6
- out_grad: bfloat16 [16384, 8, 1024], P('seq', 'head'), may hold values from -6 to 6
- doc_ids: int32 [16384], P('seq'), may hold values from 0 to 63, never falling along the last dimension, each value on 1 to 384 neighbouring positions
Outputs:
- attended: bfloat16 [16384, 8, 1024], P('seq', 'head')
- query_grad: bfloat16 [16384, 8, 1024], P('seq', 'head')
- key_grad: bfloat16 [16384, 1024], P('seq', 'head')
- value_grad: bfloat16 [16384, 1024], P('seq', 'head')
The draws below stay inside these ranges and needn't reach their ends.
Inputs may be any that keep to these rules, and one draw needn't show every extreme that they name: `doc_ids`: document ids never fall; each document has at most 384 tokens, one exactly that many.
All inputs are finite; a program needn't handle non-finite values.
Results may differ from the reference program's by a relative error of at most 0.0067.
Values may be sent and summed in bfloat16 or wider, within the bound.
No kernel may reach another device: no remote copies, remote signals or barrier semaphores. Data moves between devices by JAX's collectives and lax.ppermute only.
A program may use at most 32 MiB of HBM per device.

```python
import math
import jax
import jax.numpy as jnp
import numpy as np
from jax import lax

HD = 128
KVH = 8
REP = 8
TOK_DEV = 128
REACH = 3
TOKENS = 16384
DOCS = 64


def draw_keys(key, part):
    base = jax.random.truncated_normal(jax.random.fold_in(key, 11), -6.0, 6.0, (TOKENS, KVH, HD), jnp.float32)
    return base.reshape(TOKENS, KVH * HD).astype(jnp.bfloat16)


def draw_queries(key, part):
    base = jax.random.truncated_normal(jax.random.fold_in(key, 21), -6.0, 6.0, (TOKENS, REP, KVH, HD), jnp.float32)
    return base.reshape(TOKENS, REP, KVH * HD).astype(jnp.bfloat16)


def level_of(stream_key, dims, cuts, smallest, top_value):
    level = 1.0
    for dim, shards_of in cuts:
        heights = jax.random.uniform(jax.random.fold_in(jax.random.fold_in(stream_key, 6), dim), (shards_of,), jnp.float32, smallest / len(cuts), top_value / len(cuts))
        level = level * jnp.repeat(jnp.exp(heights), dims[dim] // shards_of).reshape((-1,) + (1,) * (len(dims) - 1 - dim))
    return level


def length_profile(count, total, most, slope):
    weights = [(1 << 20) // math.isqrt(rank ** slope) + 1 for rank in range(2, count + 1)]
    rest, holding = total - most - (count - 1), [1] * (count - 1)
    while rest > 0:
        free = [i for i in range(count - 1) if holding[i] < most]
        pool, remaining = sum([weights[i] for i in free]), rest
        for i in free:
            more = min(most - holding[i], max(1, remaining * weights[i] // pool), rest)
            holding[i] = holding[i] + more
            rest = rest - more
    return np.array([most] + holding)


def ragged_sizes(own_key, number_of, total, most, skew):
    if number_of == 2:
        one = jax.random.randint(own_key, (), max(1, total - most), min(most, total - 1) + 1)
        return jnp.stack([one, total - one])
    sizes = jnp.asarray(length_profile(number_of, total, most, skew), jnp.int32)
    twos = (number_of - 1) // 2
    donor, taker = sizes[1:1 + 2 * twos:2], sizes[2:2 + 2 * twos:2]
    margin = jnp.minimum(donor - 1, most - taker)
    shifted = jax.random.randint(jax.random.fold_in(own_key, 1), (twos,), 0, 1 << 20) % (margin + 1)
    sizes = sizes.at[1:1 + 2 * twos:2].set(donor - shifted).at[2:2 + 2 * twos:2].set(taker + shifted)
    return sizes[jax.random.permutation(jax.random.fold_in(own_key, 2), number_of)]


def scatter_about(rng, extent, scale, reach, split=(), held_as=jnp.bfloat16):
    array = scale * jax.random.normal(rng, extent, jnp.float32)
    if split:
        array = array * level_of(rng, extent, split, -0.22, 0.18)
    return jnp.clip(array, -reach, reach).astype(held_as)


def setup_inputs(seed: int = 0) -> dict:
    key_of = jax.random.split(jax.random.key(seed), 6)
    queries = draw_queries(jax.random.fold_in(key_of[5], 71), 0)
    keys = draw_keys(jax.random.fold_in(key_of[5], 71), 0)
    values = scatter_about(key_of[2], (TOKENS, KVH * HD), 1.0, 6.0, ((0, 128), (1, 8)))
    out_grad = scatter_about(key_of[3], (TOKENS, REP, KVH * HD), 1.0, 6.0, ((0, 128), (1, 8)))
    doc_ids = jnp.searchsorted(jnp.cumsum(ragged_sizes(key_of[4], DOCS, TOKENS, REACH * TOK_DEV, 2)), jnp.arange(TOKENS), side="right").astype(jnp.int32)
    return dict(queries=queries, keys=keys, values=values, out_grad=out_grad, doc_ids=doc_ids)


def window_terms(query_blk, grad_blk, key_win, value_win, seg_rows, seg_keys):
    rows_n = query_blk.shape[0]
    width = key_win.shape[0]
    scale = 1.0 / math.sqrt(HD)
    query_f = query_blk.astype(jnp.float32).reshape(rows_n, REP, KVH, HD)
    grad_f = grad_blk.astype(jnp.float32).reshape(rows_n, REP, KVH, HD)
    key_f = key_win.astype(jnp.float32).reshape(width, KVH, HD)
    value_f = value_win.astype(jnp.float32).reshape(width, KVH, HD)
    row_pos = jnp.arange(rows_n, dtype=jnp.int32)[:, None] + (width - rows_n)
    col_pos = jnp.arange(width, dtype=jnp.int32)[None, :]
    allowed = (seg_rows[:, None] == seg_keys[None, :]) & (col_pos <= row_pos)
    scores = jnp.einsum('trgd,ugd->grtu', query_f, key_f) * scale
    scores = jnp.where(allowed, scores, -1e+30)
    row_max = lax.optimization_barrier(jnp.max(scores, axis=-1, keepdims=True))
    expo = jnp.where(allowed, jnp.exp(scores - row_max), 0.0)
    probs = expo / lax.optimization_barrier(jnp.sum(expo, axis=-1, keepdims=True))
    probs_b = lax.optimization_barrier(probs.astype(jnp.bfloat16)).astype(jnp.float32)
    attended = jnp.einsum('grtu,ugd->trgd', probs_b, value_f).astype(jnp.bfloat16)
    dprob = jnp.einsum('trgd,ugd->grtu', grad_f, value_f)
    delta = lax.optimization_barrier(jnp.sum(probs * dprob, axis=-1, keepdims=True))
    dscore = lax.optimization_barrier((probs * (dprob - delta) * scale).astype(jnp.bfloat16)).astype(jnp.float32)
    query_grad = jnp.einsum('grtu,ugd->trgd', dscore, key_f).astype(jnp.bfloat16)
    key_grad = jnp.einsum('grtu,trgd->ugd', dscore, query_f)
    value_grad = jnp.einsum('grtu,trgd->ugd', probs_b, grad_f)
    return (attended.reshape(rows_n, REP, KVH * HD), query_grad.reshape(rows_n, REP, KVH * HD), key_grad.reshape(width, KVH * HD), value_grad.reshape(width, KVH * HD))

def reference(queries, keys, values, out_grad, doc_ids):
    rows_n = TOK_DEV
    blocks = TOKENS // rows_n
    width = (REACH + 1) * rows_n
    key_pad = jnp.concatenate([jnp.zeros((REACH * rows_n, KVH * HD), jnp.bfloat16), keys], axis=0)
    value_pad = jnp.concatenate([jnp.zeros((REACH * rows_n, KVH * HD), jnp.bfloat16), values], axis=0)
    seg_pad = jnp.concatenate([jnp.full((REACH * rows_n,), -1, jnp.int32), doc_ids.astype(jnp.int32)], axis=0)

    def one_block(index):
        start = (index * rows_n).astype(jnp.int32)
        query_blk = lax.dynamic_slice_in_dim(queries, start, rows_n, 0)
        grad_blk = lax.dynamic_slice_in_dim(out_grad, start, rows_n, 0)
        seg_rows = lax.dynamic_slice_in_dim(doc_ids.astype(jnp.int32), start, rows_n, 0)
        key_win = lax.dynamic_slice_in_dim(key_pad, start, width, 0)
        value_win = lax.dynamic_slice_in_dim(value_pad, start, width, 0)
        seg_keys = lax.dynamic_slice_in_dim(seg_pad, start, width, 0)
        return window_terms(query_blk, grad_blk, key_win, value_win, seg_rows, seg_keys)
    attended, query_grad, key_win_grad, value_win_grad = lax.map(one_block, jnp.arange(blocks, dtype=jnp.int32))

    def combine(window_grad):
        total = window_grad[:, REACH * rows_n:]
        for step in range(1, REACH + 1):
            piece = window_grad[step:, (REACH - step) * rows_n:(REACH - step + 1) * rows_n]
            filler = jnp.zeros((step, rows_n, KVH * HD), jnp.float32)
            total = total + jnp.concatenate([piece, filler], axis=0)
        return total.reshape(TOKENS, KVH * HD).astype(jnp.bfloat16)
    return (attended.reshape(TOKENS, REP, KVH * HD), query_grad.reshape(TOKENS, REP, KVH * HD), combine(key_win_grad), combine(value_win_grad))
```

```python
import math

import jax
import jax.numpy as jnp
from jax import lax
from jax.sharding import PartitionSpec as P

HD = 128
REACH = 3


def passed_along(value, axis, steps):
    count = lax.axis_size(axis)
    leading, last = (max(0, -steps), min(count, count - steps))
    return lax.ppermute(value, axis, [(source, source + steps) for source in range(leading, last)])


def attend(query_blk, grad_blk, key_win, value_win, seg_rows, seg_keys):
    rows_n = query_blk.shape[0]
    width = key_win.shape[0]
    scale = 1.0 / math.sqrt(HD)
    row_pos = lax.broadcasted_iota(jnp.int32, (rows_n, width), 0) + (width - rows_n)
    col_pos = lax.broadcasted_iota(jnp.int32, (rows_n, width), 1)
    allowed = (seg_rows[:, None] == seg_keys[None, :]) & (col_pos <= row_pos)
    scores = (
        jnp.einsum("trgd,ugd->grtu", query_blk, key_win, preferred_element_type=jnp.float32) * scale
    )
    scores = jnp.where(allowed, scores, -1e30)
    row_max = jnp.max(scores, axis=-1, keepdims=True)
    expo = jnp.where(allowed, jnp.exp(scores - row_max), 0.0)
    probs = expo / jnp.sum(expo, axis=-1, keepdims=True)
    probs_b = probs.astype(jnp.bfloat16)
    attended = jnp.einsum(
        "grtu,ugd->trgd", probs_b, value_win, preferred_element_type=jnp.float32
    ).astype(jnp.bfloat16)
    dprob = jnp.einsum("trgd,ugd->grtu", grad_blk, value_win, preferred_element_type=jnp.float32)
    delta = jnp.sum(probs * dprob, axis=-1, keepdims=True)
    dscore = (probs * (dprob - delta) * scale).astype(jnp.bfloat16)
    query_grad = jnp.einsum(
        "grtu,ugd->trgd", dscore, key_win, preferred_element_type=jnp.float32
    ).astype(jnp.bfloat16)
    key_grad = jnp.einsum("grtu,trgd->ugd", dscore, query_blk, preferred_element_type=jnp.float32)
    value_grad = jnp.einsum("grtu,trgd->ugd", probs_b, grad_blk, preferred_element_type=jnp.float32)
    return (attended, query_grad, key_grad, value_grad)


def on_device(queries, keys, values, out_grad, doc_ids):
    rows_n = queries.shape[0]
    reps_here = queries.shape[1]
    groups_total = queries.shape[2] // HD
    heads = lax.axis_size("head")
    groups_here = groups_total // heads
    reps_total = reps_here * heads
    width = (REACH + 1) * rows_n
    cols = groups_here * HD

    both = jnp.stack(
        [
            queries.reshape(rows_n, reps_here, groups_total, HD),
            out_grad.reshape(rows_n, reps_here, groups_total, HD),
        ]
    )
    both = lax.all_to_all(both, "head", 3, 2, tiled=True)
    query_blk, grad_blk = both[0], both[1]

    kv = jnp.concatenate([keys, values], axis=1)
    kv_cols = kv.shape[1]
    mark_rows = -(-rows_n // kv_cols)
    marks = jnp.pad((doc_ids + 1).astype(jnp.bfloat16), (0, mark_rows * kv_cols - rows_n))
    packed = jnp.concatenate([kv, marks.reshape(mark_rows, kv_cols)], axis=0)
    kv_list = []
    seg_list = []
    for step in range(REACH, 0, -1):
        got = passed_along(packed, "seq", step)
        kv_list.append(got[:rows_n])
        seg_list.append(got[rows_n:].reshape(-1)[:rows_n].astype(jnp.int32) - 1)
    kv_win = jnp.concatenate(kv_list + [kv], axis=0)
    key_win = kv_win[:, :cols].reshape(width, groups_here, HD)
    value_win = kv_win[:, cols:].reshape(width, groups_here, HD)
    seg_keys = jnp.concatenate(seg_list + [doc_ids], axis=0)

    attended, query_grad, key_grad, value_grad = attend(
        query_blk, grad_blk, key_win, value_win, doc_ids, seg_keys
    )

    out_both = jnp.stack([attended, query_grad])
    out_both = lax.all_to_all(out_both, "head", 2, 3, tiled=True)
    attended_out = out_both[0].reshape(rows_n, reps_here, groups_total * HD)
    query_out = out_both[1].reshape(rows_n, reps_here, groups_total * HD)

    grad_win = jnp.concatenate(
        [key_grad.reshape(width, cols), value_grad.reshape(width, cols)], axis=1
    )
    total = grad_win[REACH * rows_n :]
    for step in range(1, REACH + 1):
        lower = (REACH - step) * rows_n
        total = total + passed_along(grad_win[lower : lower + rows_n], "seq", -step)
    key_out = total[:, :cols].astype(jnp.bfloat16)
    value_out = total[:, cols:].astype(jnp.bfloat16)
    return (attended_out, query_out, key_out, value_out)


def solution(mesh):
    in_specs = (
        P("seq", "head", None),
        P("seq", "head"),
        P("seq", "head"),
        P("seq", "head", None),
        P("seq"),
    )
    out_specs = (P("seq", "head", None), P("seq", "head", None), P("seq", "head"), P("seq", "head"))
    return jax.shard_map(
        on_device, mesh=mesh, in_specs=in_specs, out_specs=out_specs, check_vma=False
    )
```

```python
import math

import jax
import jax.numpy as jnp
from jax import lax
from jax.sharding import PartitionSpec as P

HD = 128
REACH = 3


def passed_along(value, axis, steps):
    count = lax.axis_size(axis)
    leading, last = (max(0, -steps), min(count, count - steps))
    return lax.ppermute(value, axis, [(source, source + steps) for source in range(leading, last)])


def attend(query_blk, grad_blk, key_win, value_win, seg_rows, seg_keys):
    rows_n = query_blk.shape[2]
    width = key_win.shape[0]
    scale = 1.0 / math.sqrt(HD)
    row_pos = lax.broadcasted_iota(jnp.int32, (rows_n, width), 0) + (width - rows_n)
    col_pos = lax.broadcasted_iota(jnp.int32, (rows_n, width), 1)
    allowed = (seg_rows[:, None] == seg_keys[None, :]) & (col_pos <= row_pos)
    scores = (
        jnp.einsum("grtd,ugd->grtu", query_blk, key_win, preferred_element_type=jnp.float32) * scale
    )
    scores = jnp.where(allowed, scores, -1e30)
    row_max = jnp.max(scores, axis=-1, keepdims=True)
    expo = jnp.where(allowed, jnp.exp(scores - row_max), 0.0)
    probs = expo / jnp.sum(expo, axis=-1, keepdims=True)
    probs_b = probs.astype(jnp.bfloat16)
    attended = jnp.einsum(
        "grtu,ugd->grtd", probs_b, value_win, preferred_element_type=jnp.float32
    ).astype(jnp.bfloat16)
    dprob = jnp.einsum("grtd,ugd->grtu", grad_blk, value_win, preferred_element_type=jnp.float32)
    delta = jnp.sum(probs * dprob, axis=-1, keepdims=True)
    dscore = (probs * (dprob - delta) * scale).astype(jnp.bfloat16)
    query_grad = jnp.einsum(
        "grtu,ugd->grtd", dscore, key_win, preferred_element_type=jnp.float32
    ).astype(jnp.bfloat16)
    key_grad = jnp.einsum("grtu,grtd->ugd", dscore, query_blk, preferred_element_type=jnp.float32)
    value_grad = jnp.einsum("grtu,grtd->ugd", probs_b, grad_blk, preferred_element_type=jnp.float32)
    return (attended, query_grad, key_grad, value_grad)


def on_device(queries, keys, values, out_grad, doc_ids):
    rows_n = queries.shape[0]
    reps_here = queries.shape[1]
    groups_total = queries.shape[2] // HD
    heads = lax.axis_size("head")
    groups_here = groups_total // heads
    reps_total = reps_here * heads
    width = (REACH + 1) * rows_n
    cols = groups_here * HD

    both = jnp.stack(
        [
            queries.reshape(rows_n, reps_here, groups_total, HD),
            out_grad.reshape(rows_n, reps_here, groups_total, HD),
        ],
        axis=0,
    ).transpose(3, 0, 2, 1, 4)
    both = lax.all_to_all(both, "head", 0, 0, tiled=True)
    both = both.reshape(heads, groups_here, 2, reps_here, rows_n, HD).transpose(2, 1, 0, 3, 4, 5)
    both = both.reshape(2, groups_here, reps_total, rows_n, HD)
    query_blk, grad_blk = both[0], both[1]

    mark_rows = -(-rows_n // cols)
    marks = jnp.pad((doc_ids + 1).astype(jnp.bfloat16), (0, mark_rows * cols - rows_n))
    packed = jnp.concatenate([keys, values, marks.reshape(mark_rows, cols)], axis=0)
    key_list = []
    value_list = []
    seg_list = []
    for step in range(REACH, 0, -1):
        got = passed_along(packed, "seq", step)
        key_list.append(got[:rows_n])
        value_list.append(got[rows_n : 2 * rows_n])
        seg_list.append(got[2 * rows_n :].reshape(-1)[:rows_n].astype(jnp.int32) - 1)
    key_win = jnp.concatenate(key_list + [keys], axis=0).reshape(width, groups_here, HD)
    value_win = jnp.concatenate(value_list + [values], axis=0).reshape(width, groups_here, HD)
    seg_keys = jnp.concatenate(seg_list + [doc_ids], axis=0)

    attended, query_grad, key_grad, value_grad = attend(
        query_blk, grad_blk, key_win, value_win, doc_ids, seg_keys
    )

    out_both = jnp.stack([attended, query_grad], axis=0)
    out_both = out_both.reshape(2, groups_here, heads, reps_here, rows_n, HD).transpose(2, 1, 0, 3, 4, 5)
    out_both = out_both.reshape(heads * groups_here, 2, reps_here, rows_n, HD)
    out_both = lax.all_to_all(out_both, "head", 0, 0, tiled=True)
    out_both = out_both.transpose(1, 3, 2, 0, 4).reshape(2, rows_n, reps_here, groups_total * HD)
    attended_out, query_out = out_both[0], out_both[1]

    key_grad = key_grad.reshape(width, cols)
    value_grad = value_grad.reshape(width, cols)
    total_keys = key_grad[REACH * rows_n :]
    total_values = value_grad[REACH * rows_n :]
    for step in range(1, REACH + 1):
        lower = (REACH - step) * rows_n
        back = passed_along(
            jnp.concatenate(
                [key_grad[lower : lower + rows_n], value_grad[lower : lower + rows_n]], axis=0
            ),
            "seq",
            -step,
        )
        total_keys = total_keys + back[:rows_n]
        total_values = total_values + back[rows_n:]
    return (attended_out, query_out, total_keys.astype(jnp.bfloat16), total_values.astype(jnp.bfloat16))


def solution(mesh):
    in_specs = (
        P("seq", "head", None),
        P("seq", "head"),
        P("seq", "head"),
        P("seq", "head", None),
        P("seq"),
    )
    out_specs = (P("seq", "head", None), P("seq", "head", None), P("seq", "head"), P("seq", "head"))
    return jax.shard_map(
        on_device, mesh=mesh, in_specs=in_specs, out_specs=out_specs, check_vma=False
    )
```

```python
import math

import jax
import jax.numpy as jnp
from jax import lax
from jax.experimental import pallas as pl
from jax.sharding import PartitionSpec as P

HD = 128
REACH = 3
INTERPRET = False


def passed_along(value, axis, steps):
    count = lax.axis_size(axis)
    leading, last = (max(0, -steps), min(count, count - steps))
    return lax.ppermute(value, axis, [(source, source + steps) for source in range(leading, last)])


def _full(shape):
    return pl.BlockSpec(shape, lambda: (0,) * len(shape))


def relay_in_kernel(q_ref, d_ref, o_ref):
    for g in range(o_ref.shape[0]):
        o_ref[g, 0] = q_ref[:, g * HD : (g + 1) * HD]
        o_ref[g, 1] = d_ref[:, g * HD : (g + 1) * HD]


def relay_in(q2, d2):
    rows_n, width = q2.shape
    shape = (width // HD, 2, rows_n, HD)
    return pl.pallas_call(
        relay_in_kernel,
        out_shape=jax.ShapeDtypeStruct(shape, q2.dtype),
        in_specs=[_full(q2.shape), _full(d2.shape)],
        out_specs=_full(shape),
        interpret=INTERPRET,
    )(q2, d2)


def relay_out_kernel(x_ref, a_ref, q_ref):
    for g in range(x_ref.shape[0]):
        a_ref[:, g * HD : (g + 1) * HD] = x_ref[g, 0]
        q_ref[:, g * HD : (g + 1) * HD] = x_ref[g, 1]


def relay_out(x):
    groups, _, rows_n, _ = x.shape
    shape = (rows_n, groups * HD)
    return pl.pallas_call(
        relay_out_kernel,
        out_shape=(jax.ShapeDtypeStruct(shape, x.dtype), jax.ShapeDtypeStruct(shape, x.dtype)),
        in_specs=[_full(x.shape)],
        out_specs=(_full(shape), _full(shape)),
        interpret=INTERPRET,
    )(x)


def attend_kernel(x_ref, k_ref, v_ref, segk_ref, segr_ref, y_ref, dkv_ref):
    reps, _, rows_n, _ = x_ref.shape
    width = k_ref.shape[0]
    scale = 1.0 / math.sqrt(HD)
    key_win = k_ref[...]
    value_win = v_ref[...]
    row_pos = lax.broadcasted_iota(jnp.int32, (rows_n, width), 0) + (width - rows_n)
    col_pos = lax.broadcasted_iota(jnp.int32, (rows_n, width), 1)
    allowed = (segr_ref[...] == segk_ref[...]) & (col_pos <= row_pos)
    on_minor = (((1,), (1,)), ((), ()))
    on_major = (((0,), (0,)), ((), ()))
    key_grad = jnp.zeros((width, HD), jnp.float32)
    value_grad = jnp.zeros((width, HD), jnp.float32)
    for r in range(reps):
        query = x_ref[r, 0]
        grad = x_ref[r, 1]
        scores = lax.dot_general(query, key_win, on_minor, preferred_element_type=jnp.float32) * scale
        scores = jnp.where(allowed, scores, -1e30)
        row_max = jnp.max(scores, axis=-1, keepdims=True)
        expo = jnp.where(allowed, jnp.exp(scores - row_max), 0.0)
        probs = expo / jnp.sum(expo, axis=-1, keepdims=True)
        probs_b = probs.astype(jnp.bfloat16)
        y_ref[r, 0] = jnp.dot(probs_b, value_win, preferred_element_type=jnp.float32).astype(
            jnp.bfloat16
        )
        dprob = lax.dot_general(grad, value_win, on_minor, preferred_element_type=jnp.float32)
        delta = jnp.sum(probs * dprob, axis=-1, keepdims=True)
        dscore = (probs * (dprob - delta) * scale).astype(jnp.bfloat16)
        y_ref[r, 1] = jnp.dot(dscore, key_win, preferred_element_type=jnp.float32).astype(
            jnp.bfloat16
        )
        key_grad = key_grad + lax.dot_general(
            dscore, query, on_major, preferred_element_type=jnp.float32
        )
        value_grad = value_grad + lax.dot_general(
            probs_b, grad, on_major, preferred_element_type=jnp.float32
        )
    for b in range(width // rows_n):
        dkv_ref[b, 0] = key_grad[b * rows_n : (b + 1) * rows_n]
        dkv_ref[b, 1] = value_grad[b * rows_n : (b + 1) * rows_n]


def attend(x, key_win, value_win, seg_keys, seg_rows):
    reps, _, rows_n, _ = x.shape
    width = key_win.shape[0]
    y_shape = x.shape
    dkv_shape = (width // rows_n, 2, rows_n, HD)
    cost = pl.CostEstimate(
        flops=12 * reps * rows_n * width * HD,
        transcendentals=reps * rows_n * width,
        bytes_accessed=2 * 2 * x.size + 2 * 2 * key_win.size + 4 * 2 * width * HD,
    )
    return pl.pallas_call(
        attend_kernel,
        out_shape=(
            jax.ShapeDtypeStruct(y_shape, jnp.bfloat16),
            jax.ShapeDtypeStruct(dkv_shape, jnp.float32),
        ),
        in_specs=[
            _full(x.shape),
            _full(key_win.shape),
            _full(value_win.shape),
            _full(seg_keys.shape),
            _full(seg_rows.shape),
        ],
        out_specs=(_full(y_shape), _full(dkv_shape)),
        cost_estimate=cost,
        interpret=INTERPRET,
    )(x, key_win, value_win, seg_keys, seg_rows)


def on_device(queries, keys, values, out_grad, doc_ids):
    rows_n = queries.shape[0]
    groups_total = queries.shape[2] // HD
    heads = lax.axis_size("head")
    assert queries.shape[1] == 1 and keys.shape[1] == HD and groups_total == heads

    both = relay_in(
        queries.reshape(rows_n, groups_total * HD), out_grad.reshape(rows_n, groups_total * HD)
    )
    both = lax.all_to_all(both, "head", 0, 0, tiled=True)

    mark_rows = -(-rows_n // HD)
    marks = jnp.pad((doc_ids + 1).astype(jnp.bfloat16), (0, mark_rows * HD - rows_n))
    packed = jnp.concatenate([keys, values, marks.reshape(mark_rows, HD)], axis=0)
    key_list = []
    value_list = []
    seg_list = []
    for step in range(REACH, 0, -1):
        got = passed_along(packed, "seq", step)
        key_list.append(got[:rows_n])
        value_list.append(got[rows_n : 2 * rows_n])
        seg_list.append(got[2 * rows_n :].reshape(-1)[:rows_n].astype(jnp.int32) - 1)
    key_win = jnp.concatenate(key_list + [keys], axis=0)
    value_win = jnp.concatenate(value_list + [values], axis=0)
    seg_keys = jnp.concatenate(seg_list + [doc_ids], axis=0)

    out_both, grad_win = attend(
        both, key_win, value_win, seg_keys.reshape(1, -1), doc_ids.reshape(rows_n, 1)
    )

    out_both = lax.all_to_all(out_both, "head", 0, 0, tiled=True)
    attended_out, query_out = relay_out(out_both)

    total = grad_win[REACH]
    for step in range(1, REACH + 1):
        total = total + passed_along(grad_win[REACH - step], "seq", -step)
    return (
        attended_out.reshape(queries.shape),
        query_out.reshape(queries.shape),
        total[0].astype(jnp.bfloat16),
        total[1].astype(jnp.bfloat16),
    )


def solution(mesh):
    in_specs = (
        P("seq", "head", None),
        P("seq", "head"),
        P("seq", "head"),
        P("seq", "head", None),
        P("seq"),
    )
    out_specs = (P("seq", "head", None), P("seq", "head", None), P("seq", "head"), P("seq", "head"))
    return jax.shard_map(
        on_device, mesh=mesh, in_specs=in_specs, out_specs=out_specs, check_vma=False
    )
```

```python
import math

import jax
import jax.numpy as jnp
from jax import lax
from jax.experimental import pallas as pl
from jax.experimental.pallas import tpu as pltpu
from jax.sharding import PartitionSpec as P

HD = 128
REACH = 3
INTERPRET = False


def passed_along(value, axis, steps):
    count = lax.axis_size(axis)
    leading, last = (max(0, -steps), min(count, count - steps))
    return lax.ppermute(value, axis, [(source, source + steps) for source in range(leading, last)])


def _full(shape):
    return pl.BlockSpec(shape, lambda: (0,) * len(shape))


_HBM = pl.BlockSpec(memory_space=pl.ANY)


def relay_in_kernel(q_hbm, d_hbm, o_hbm, sems):
    groups = o_hbm.shape[0]
    copies = []
    for g in range(groups):
        for which, src in enumerate((q_hbm, d_hbm)):
            copies.append(
                pltpu.make_async_copy(
                    src.at[:, pl.ds(g * HD, HD)], o_hbm.at[g, which], sems.at[2 * g + which]
                )
            )
    for c in copies:
        c.start()
    for c in copies:
        c.wait()


def relay_in(q2, d2):
    rows_n, width = q2.shape
    groups = width // HD
    shape = (groups, 2, rows_n, HD)
    return pl.pallas_call(
        relay_in_kernel,
        out_shape=jax.ShapeDtypeStruct(shape, q2.dtype),
        in_specs=[_HBM, _HBM],
        out_specs=_HBM,
        scratch_shapes=[pltpu.SemaphoreType.DMA((2 * groups,))],
        interpret=INTERPRET,
    )(q2, d2)


def relay_out_kernel(x_hbm, a_hbm, q_hbm, sems):
    groups = x_hbm.shape[0]
    copies = []
    for g in range(groups):
        for which, dst in enumerate((a_hbm, q_hbm)):
            copies.append(
                pltpu.make_async_copy(
                    x_hbm.at[g, which], dst.at[:, pl.ds(g * HD, HD)], sems.at[2 * g + which]
                )
            )
    for c in copies:
        c.start()
    for c in copies:
        c.wait()


def relay_out(x):
    groups, _, rows_n, _ = x.shape
    shape = (rows_n, groups * HD)
    return pl.pallas_call(
        relay_out_kernel,
        out_shape=(jax.ShapeDtypeStruct(shape, x.dtype), jax.ShapeDtypeStruct(shape, x.dtype)),
        in_specs=[_HBM],
        out_specs=(_HBM, _HBM),
        scratch_shapes=[pltpu.SemaphoreType.DMA((2 * groups,))],
        interpret=INTERPRET,
    )(x)


def attend_kernel(x_ref, k_ref, v_ref, segk_ref, segr_ref, y_ref, dkv_ref):
    reps, _, rows_n, _ = x_ref.shape
    width = k_ref.shape[0]
    scale = 1.0 / math.sqrt(HD)
    key_win = k_ref[...]
    value_win = v_ref[...]
    key_t = key_win.T
    value_t = value_win.T
    row_pos = lax.broadcasted_iota(jnp.int32, (rows_n, width), 0) + (width - rows_n)
    col_pos = lax.broadcasted_iota(jnp.int32, (rows_n, width), 1)
    allowed = (segr_ref[...] == segk_ref[...]) & (col_pos <= row_pos)
    on_major = (((0,), (0,)), ((), ()))
    key_grad_t = jnp.zeros((HD, width), jnp.float32)
    value_grad_t = jnp.zeros((HD, width), jnp.float32)
    for r in range(reps):
        query = x_ref[r, 0]
        grad = x_ref[r, 1]
        scores = jnp.dot(query, key_t, preferred_element_type=jnp.float32) * scale
        scores = jnp.where(allowed, scores, -1e30)
        row_max = jnp.max(scores, axis=-1, keepdims=True)
        expo = jnp.where(allowed, jnp.exp(scores - row_max), 0.0)
        probs = expo / jnp.sum(expo, axis=-1, keepdims=True)
        probs_b = probs.astype(jnp.bfloat16)
        y_ref[r, 0] = jnp.dot(probs_b, value_win, preferred_element_type=jnp.float32).astype(
            jnp.bfloat16
        )
        dprob = jnp.dot(grad, value_t, preferred_element_type=jnp.float32)
        delta = jnp.sum(probs * dprob, axis=-1, keepdims=True)
        dscore = (probs * (dprob - delta) * scale).astype(jnp.bfloat16)
        y_ref[r, 1] = jnp.dot(dscore, key_win, preferred_element_type=jnp.float32).astype(
            jnp.bfloat16
        )
        key_grad_t = key_grad_t + lax.dot_general(
            query, dscore, on_major, preferred_element_type=jnp.float32
        )
        value_grad_t = value_grad_t + lax.dot_general(
            grad, probs_b, on_major, preferred_element_type=jnp.float32
        )
    for b in range(width // rows_n):
        dkv_ref[b, 0] = key_grad_t[:, b * rows_n : (b + 1) * rows_n].T
        dkv_ref[b, 1] = value_grad_t[:, b * rows_n : (b + 1) * rows_n].T


def attend(x, key_win, value_win, seg_keys, seg_rows):
    reps, _, rows_n, _ = x.shape
    width = key_win.shape[0]
    y_shape = x.shape
    dkv_shape = (width // rows_n, 2, rows_n, HD)
    cost = pl.CostEstimate(
        flops=12 * reps * rows_n * width * HD,
        transcendentals=reps * rows_n * width,
        bytes_accessed=2 * 2 * x.size + 2 * 2 * key_win.size + 4 * 2 * width * HD,
    )
    return pl.pallas_call(
        attend_kernel,
        out_shape=(
            jax.ShapeDtypeStruct(y_shape, jnp.bfloat16),
            jax.ShapeDtypeStruct(dkv_shape, jnp.float32),
        ),
        in_specs=[
            _full(x.shape),
            _full(key_win.shape),
            _full(value_win.shape),
            _full(seg_keys.shape),
            _full(seg_rows.shape),
        ],
        out_specs=(_full(y_shape), _full(dkv_shape)),
        cost_estimate=cost,
        interpret=INTERPRET,
    )(x, key_win, value_win, seg_keys, seg_rows)


def on_device(queries, keys, values, out_grad, doc_ids):
    rows_n = queries.shape[0]
    groups_total = queries.shape[2] // HD
    heads = lax.axis_size("head")
    assert queries.shape[1] == 1 and keys.shape[1] == HD and groups_total == heads

    both = relay_in(
        queries.reshape(rows_n, groups_total * HD), out_grad.reshape(rows_n, groups_total * HD)
    )
    both = lax.all_to_all(both, "head", 0, 0, tiled=True)

    mark_rows = -(-rows_n // HD)
    marks = jnp.pad((doc_ids + 1).astype(jnp.bfloat16), (0, mark_rows * HD - rows_n))
    packed = jnp.concatenate([keys, values, marks.reshape(mark_rows, HD)], axis=0)
    key_list = []
    value_list = []
    seg_list = []
    for step in range(REACH, 0, -1):
        got = passed_along(packed, "seq", step)
        key_list.append(got[:rows_n])
        value_list.append(got[rows_n : 2 * rows_n])
        seg_list.append(got[2 * rows_n :].reshape(-1)[:rows_n].astype(jnp.int32) - 1)
    key_win = jnp.concatenate(key_list + [keys], axis=0)
    value_win = jnp.concatenate(value_list + [values], axis=0)
    seg_keys = jnp.concatenate(seg_list + [doc_ids], axis=0)

    out_both, grad_win = attend(
        both, key_win, value_win, seg_keys.reshape(1, -1), doc_ids.reshape(rows_n, 1)
    )

    out_both = lax.all_to_all(out_both, "head", 0, 0, tiled=True)
    attended_out, query_out = relay_out(out_both)

    total = grad_win[REACH]
    for step in range(1, REACH + 1):
        total = total + passed_along(grad_win[REACH - step], "seq", -step)
    return (
        attended_out.reshape(queries.shape),
        query_out.reshape(queries.shape),
        total[0].astype(jnp.bfloat16),
        total[1].astype(jnp.bfloat16),
    )


def solution(mesh):
    in_specs = (
        P("seq", "head", None),
        P("seq", "head"),
        P("seq", "head"),
        P("seq", "head", None),
        P("seq"),
    )
    out_specs = (P("seq", "head", None), P("seq", "head", None), P("seq", "head"), P("seq", "head"))
    return jax.shard_map(
        on_device, mesh=mesh, in_specs=in_specs, out_specs=out_specs, check_vma=False
    )
```

```python
import math

import jax
import jax.numpy as jnp
from jax import lax
from jax.sharding import PartitionSpec as P

HD = 128
REACH = 3


def passed_along(value, axis, steps):
    count = lax.axis_size(axis)
    leading, last = (max(0, -steps), min(count, count - steps))
    return lax.ppermute(value, axis, [(source, source + steps) for source in range(leading, last)])


def attend(query_blk, grad_blk, key_win, value_win, seg_rows, seg_keys):
    rows_n = query_blk.shape[0]
    width = key_win.shape[0]
    scale = 1.0 / math.sqrt(HD)
    row_pos = lax.broadcasted_iota(jnp.int32, (rows_n, width), 0) + (width - rows_n)
    col_pos = lax.broadcasted_iota(jnp.int32, (rows_n, width), 1)
    allowed = (seg_rows[:, None] == seg_keys[None, :]) & (col_pos <= row_pos)
    scores = (
        jnp.einsum("trgd,ugd->grtu", query_blk, key_win, preferred_element_type=jnp.float32) * scale
    )
    scores = jnp.where(allowed, scores, -1e30)
    row_max = jnp.max(scores, axis=-1, keepdims=True)
    expo = jnp.where(allowed, jnp.exp(scores - row_max), 0.0)
    probs = expo / jnp.sum(expo, axis=-1, keepdims=True)
    probs_b = probs.astype(jnp.bfloat16)
    attended = jnp.einsum(
        "grtu,ugd->trgd", probs_b, value_win, preferred_element_type=jnp.float32
    ).astype(jnp.bfloat16)
    dprob = jnp.einsum("trgd,ugd->grtu", grad_blk, value_win, preferred_element_type=jnp.float32)
    delta = jnp.sum(probs * dprob, axis=-1, keepdims=True)
    dscore = (probs * (dprob - delta) * scale).astype(jnp.bfloat16)
    query_grad = jnp.einsum(
        "grtu,ugd->trgd", dscore, key_win, preferred_element_type=jnp.float32
    ).astype(jnp.bfloat16)
    key_grad = jnp.einsum("grtu,trgd->ugd", dscore, query_blk, preferred_element_type=jnp.float32)
    value_grad = jnp.einsum("grtu,trgd->ugd", probs_b, grad_blk, preferred_element_type=jnp.float32)
    return (attended, query_grad, key_grad, value_grad)


def on_device(queries, keys, values, out_grad, doc_ids):
    rows_n = queries.shape[0]
    reps_here = queries.shape[1]
    groups_total = queries.shape[2] // HD
    heads = lax.axis_size("head")
    groups_here = groups_total // heads
    reps_total = reps_here * heads
    width = (REACH + 1) * rows_n
    cols = groups_here * HD

    both = jnp.stack(
        [
            queries.reshape(rows_n, reps_here, groups_total, HD),
            out_grad.reshape(rows_n, reps_here, groups_total, HD),
        ]
    )
    both = lax.all_to_all(both, "head", 3, 2, tiled=True)
    query_blk, grad_blk = both[0], both[1]

    kv = jnp.concatenate([keys, values], axis=1)
    kv_cols = kv.shape[1]
    mark_rows = -(-rows_n // kv_cols)
    marks = jnp.pad((doc_ids + 1).astype(jnp.bfloat16), (0, mark_rows * kv_cols - rows_n))
    packed = jnp.concatenate([kv, marks.reshape(mark_rows, kv_cols)], axis=0)
    kv_list = []
    seg_list = []
    for step in range(REACH, 0, -1):
        got = passed_along(packed, "seq", step)
        kv_list.append(got[:rows_n])
        seg_list.append(got[rows_n:].reshape(-1)[:rows_n].astype(jnp.int32) - 1)
    kv_win = jnp.concatenate(kv_list + [kv], axis=0)
    key_win = kv_win[:, :cols].reshape(width, groups_here, HD)
    value_win = kv_win[:, cols:].reshape(width, groups_here, HD)
    seg_keys = jnp.concatenate(seg_list + [doc_ids], axis=0)

    block_last = seg_keys.reshape(REACH + 1, rows_n)[:REACH, -1]
    skipped = jnp.sum((block_last < doc_ids[0]).astype(jnp.int32))

    def from_block(first):
        def run(query_blk, grad_blk, key_win, value_win, seg_keys):
            lower = first * rows_n
            att, qg, kg, vg = attend(
                query_blk, grad_blk, key_win[lower:], value_win[lower:], doc_ids, seg_keys[lower:]
            )
            pad = ((lower, 0), (0, 0), (0, 0))
            return att, qg, jnp.pad(kg, pad), jnp.pad(vg, pad)

        return run

    attended, query_grad, key_grad, value_grad = lax.switch(
        skipped,
        [from_block(first) for first in range(REACH + 1)],
        query_blk,
        grad_blk,
        key_win,
        value_win,
        seg_keys,
    )

    out_both = jnp.stack([attended, query_grad])
    out_both = lax.all_to_all(out_both, "head", 2, 3, tiled=True)
    attended_out = out_both[0].reshape(rows_n, reps_here, groups_total * HD)
    query_out = out_both[1].reshape(rows_n, reps_here, groups_total * HD)

    grad_win = jnp.concatenate(
        [key_grad.reshape(width, cols), value_grad.reshape(width, cols)], axis=1
    )
    total = grad_win[REACH * rows_n :]
    for step in range(1, REACH + 1):
        lower = (REACH - step) * rows_n
        total = total + passed_along(grad_win[lower : lower + rows_n], "seq", -step)
    key_out = total[:, :cols].astype(jnp.bfloat16)
    value_out = total[:, cols:].astype(jnp.bfloat16)
    return (attended_out, query_out, key_out, value_out)


def solution(mesh):
    in_specs = (
        P("seq", "head", None),
        P("seq", "head"),
        P("seq", "head"),
        P("seq", "head", None),
        P("seq"),
    )
    out_specs = (P("seq", "head", None), P("seq", "head", None), P("seq", "head"), P("seq", "head"))
    return jax.shard_map(
        on_device, mesh=mesh, in_specs=in_specs, out_specs=out_specs, check_vma=False
    )
```

```python
import math

import jax
import jax.numpy as jnp
from jax import lax
from jax.sharding import PartitionSpec as P

HD = 128
REACH = 3


def passed_along(value, axis, steps):
    count = lax.axis_size(axis)
    leading, last = (max(0, -steps), min(count, count - steps))
    return lax.ppermute(value, axis, [(source, source + steps) for source in range(leading, last)])


def attend(query_blk, grad_blk, key_win, value_win, seg_rows, seg_keys):
    rows_n = query_blk.shape[0]
    width = key_win.shape[0]
    scale = 1.0 / math.sqrt(HD)
    row_pos = lax.broadcasted_iota(jnp.int32, (rows_n, width), 0) + (width - rows_n)
    col_pos = lax.broadcasted_iota(jnp.int32, (rows_n, width), 1)
    allowed = (seg_rows[:, None] == seg_keys[None, :]) & (col_pos <= row_pos)
    scores = (
        jnp.einsum("trgd,ugd->grtu", query_blk, key_win, preferred_element_type=jnp.float32) * scale
    )
    scores = jnp.where(allowed, scores, -1e30)
    row_max = jnp.max(scores, axis=-1, keepdims=True)
    expo = jnp.where(allowed, jnp.exp(scores - row_max), 0.0)
    probs = expo / jnp.sum(expo, axis=-1, keepdims=True)
    probs_b = probs.astype(jnp.bfloat16)
    attended = jnp.einsum(
        "grtu,ugd->trgd", probs_b, value_win, preferred_element_type=jnp.float32
    ).astype(jnp.bfloat16)
    dprob = jnp.einsum("trgd,ugd->grtu", grad_blk, value_win, preferred_element_type=jnp.float32)
    delta = jnp.sum(probs * dprob, axis=-1, keepdims=True)
    dscore = (probs * (dprob - delta) * scale).astype(jnp.bfloat16)
    query_grad = jnp.einsum(
        "grtu,ugd->trgd", dscore, key_win, preferred_element_type=jnp.float32
    ).astype(jnp.bfloat16)
    key_grad = jnp.einsum("grtu,trgd->ugd", dscore, query_blk, preferred_element_type=jnp.float32)
    value_grad = jnp.einsum("grtu,trgd->ugd", probs_b, grad_blk, preferred_element_type=jnp.float32)
    return (attended, query_grad, key_grad, value_grad)


def on_device(queries, keys, values, out_grad, doc_ids):
    rows_n = queries.shape[0]
    reps_here = queries.shape[1]
    groups_total = queries.shape[2] // HD
    heads = lax.axis_size("head")
    groups_here = groups_total // heads
    reps_total = reps_here * heads
    width = (REACH + 1) * rows_n
    cols = groups_here * HD

    both = jnp.stack(
        [
            queries.reshape(rows_n, reps_here, groups_total, HD),
            out_grad.reshape(rows_n, reps_here, groups_total, HD),
        ]
    )
    both = lax.all_to_all(both, "head", 3, 2, tiled=True)
    query_blk, grad_blk = both[0], both[1]

    kv = jnp.concatenate([keys, values], axis=1)
    kv_cols = kv.shape[1]
    mark_rows = -(-rows_n // kv_cols)
    marks = jnp.pad((doc_ids + 1).astype(jnp.bfloat16), (0, mark_rows * kv_cols - rows_n))
    packed = jnp.concatenate([kv, marks.reshape(mark_rows, kv_cols)], axis=0)
    kv_list = []
    seg_list = []
    for step in range(REACH, 0, -1):
        got = passed_along(packed, "seq", step)
        kv_list.append(got[:rows_n])
        seg_list.append(got[rows_n:].reshape(-1)[:rows_n].astype(jnp.int32) - 1)
    kv_win = jnp.concatenate(kv_list + [kv], axis=0)
    key_win = kv_win[:, :cols].reshape(width, groups_here, HD)
    value_win = kv_win[:, cols:].reshape(width, groups_here, HD)
    seg_keys = jnp.concatenate(seg_list + [doc_ids], axis=0)

    block_last = seg_keys.reshape(REACH + 1, rows_n)[:REACH, -1]
    skipped = jnp.sum((block_last < doc_ids[0]).astype(jnp.int32))

    def from_block(first):
        def run(query_blk, grad_blk, key_win, value_win, seg_keys):
            lower = first * rows_n
            att, qg, kg, vg = attend(
                query_blk, grad_blk, key_win[lower:], value_win[lower:], doc_ids, seg_keys[lower:]
            )
            pad = ((lower, 0), (0, 0), (0, 0))
            return att, qg, jnp.pad(kg, pad), jnp.pad(vg, pad)

        return run

    attended, query_grad, key_grad, value_grad = lax.switch(
        skipped,
        [from_block(first) for first in range(REACH + 1)],
        query_blk,
        grad_blk,
        key_win,
        value_win,
        seg_keys,
    )

    out_both = jnp.stack([attended, query_grad])
    out_both = lax.all_to_all(out_both, "head", 2, 3, tiled=True)
    attended_out = out_both[0].reshape(rows_n, reps_here, groups_total * HD)
    query_out = out_both[1].reshape(rows_n, reps_here, groups_total * HD)

    grad_win = jnp.concatenate(
        [key_grad.reshape(width, cols), value_grad.reshape(width, cols)], axis=1
    )
    total = grad_win[REACH * rows_n :]
    for step in range(1, REACH + 1):
        lower = (REACH - step) * rows_n
        piece = grad_win[lower : lower + rows_n].astype(jnp.bfloat16)
        total = total + passed_along(piece, "seq", -step).astype(jnp.float32)
    key_out = total[:, :cols].astype(jnp.bfloat16)
    value_out = total[:, cols:].astype(jnp.bfloat16)
    return (attended_out, query_out, key_out, value_out)


def solution(mesh):
    in_specs = (
        P("seq", "head", None),
        P("seq", "head"),
        P("seq", "head"),
        P("seq", "head", None),
        P("seq"),
    )
    out_specs = (P("seq", "head", None), P("seq", "head", None), P("seq", "head"), P("seq", "head"))
    return jax.shard_map(
        on_device, mesh=mesh, in_specs=in_specs, out_specs=out_specs, check_vma=False
    )
```
